128 devices in a mesh: sens: 8 (over y, core), tm: 16 (over z, x).
Axes of the slice: x: 4, y: 4, z: 4, core: 2. Of those that a mesh axis runs over, the one named last changes fastest.
Arguments:
- observations: bfloat16 [131072, 4096], P('sens', 'tm'), may hold values from -6 to 6
- loadings: float32 [131072, 128], P('sens'), may hold values from -6 to 6
- noise_var: float32 [131072], P('sens'), may hold values from 0.25 to 4
- decay: float32 [4096, 128], P('tm'), may hold values from 0.4 to 1
- tiles: int32 [12288, 2], replicated, may hold values from 0 to 1023, as said below
Outputs:
- new_loadings: float32 [131072, 128], P(('sens', 'tm'))
- new_noise: float32 [131072], P(('sens', 'tm'))
The draws below stay inside these ranges and needn't reach their ends.
Inputs may be any that keep to these rules, and one draw needn't show every extreme that they name: `tiles`: every pair is a distinct tile; every sensor block appears in at least one pair; the second entry is below 16.
All inputs are finite; a program needn't handle non-finite values.
Results may differ from the reference program's by a relative error of at most 0.0059.
Values may be sent and summed in bfloat16 or wider, within the bound.
No kernel may reach another device: no remote copies, remote signals or barrier semaphores. Data moves between devices by JAX's collectives and lax.ppermute only.
A program may use at most 128 MiB of HBM per device.

```python
import math
import jax
import jax.numpy as jnp
from jax import lax

FACTORS = 128
BLOCK = 128
WINDOW = 256
SENSORS = 131072
HORIZON_LENGTH = 4096
BLOCKS = 1024
WINDOWS = 16
TILES_OBS = 12288


def draw_decay(key, part):
    gradual_seed, quick_seed, extended_seed, perturbation_seed, spike_seed, survival_seed = jax.random.split(key, 6)
    slow_mask = jax.random.uniform(gradual_seed, (FACTORS,)) < 0.5
    fast_rate = jnp.exp(jax.random.uniform(quick_seed, (FACTORS,), jnp.float32, math.log(1.0 / 50.0), math.log(1.0 / 30.0)))
    long_rate = jnp.exp(jax.random.uniform(extended_seed, (FACTORS,), jnp.float32, math.log(0.05 / HORIZON_LENGTH), math.log(0.5 / HORIZON_LENGTH)))
    background_intensity = jnp.where(slow_mask, long_rate, fast_rate)
    stochastic_perturbation = jnp.exp(jax.random.uniform(perturbation_seed, (HORIZON_LENGTH, FACTORS), jnp.float32, -0.35, 0.35))
    spike_occurrences = jax.random.uniform(spike_seed, (HORIZON_LENGTH, 1)) < 3.0 / HORIZON_LENGTH
    surviving_fraction = jax.random.uniform(survival_seed, (HORIZON_LENGTH, FACTORS), jnp.float32, 0.5, 0.8)
    return jnp.exp(-background_intensity[None, :] * stochastic_perturbation) * jnp.where(spike_occurrences, surviving_fraction, 1.0)


def draw_tiles(key, part):
    key_anchor, key_tilt, key_score = jax.random.split(key, 3)
    anchor = jax.random.randint(key_anchor, (BLOCKS,), 0, WINDOWS)
    tilt_bias = jax.random.randint(key_tilt, (BLOCKS,), 0, 4)
    scores = jax.random.randint(key_score, (BLOCKS, WINDOWS), 0, 16) + 8 * tilt_bias[:, None]
    scores = jnp.where(jnp.arange(WINDOWS)[None, :] == anchor[:, None], 1000, scores)
    ranked = scores.reshape(-1) * (BLOCKS * WINDOWS) + jnp.arange(BLOCKS * WINDOWS)
    _, picked = lax.top_k(ranked, TILES_OBS)
    return jnp.stack([picked // WINDOWS, picked % WINDOWS], axis=1).astype(jnp.int32)


def steps_of(rng, dims, pieces, smallest, high):
    level = 1.0
    for axis_at, blocks in pieces:
        steps = jax.random.uniform(jax.random.fold_in(jax.random.fold_in(rng, 6), axis_at), (blocks,), jnp.float32, smallest / len(pieces), high / len(pieces))
        level = level * jnp.repeat(jnp.exp(steps), dims[axis_at] // blocks).reshape((-1,) + (1,) * (len(dims) - 1 - axis_at))
    return level


def centred(stream_key, dims, spread, bound, shards=(), kind=jnp.bfloat16):
    entries = jax.random.normal(stream_key, dims, jnp.float32) * spread
    if len(shards) > 0:
        entries = steps_of(stream_key, dims, shards, -0.22, 0.18) * entries
    return jnp.clip(entries, min=-bound, max=bound).astype(kind)


def setup_inputs(seed: int = 0) -> dict:
    seeds = jax.random.split(jax.random.key(seed), 6)
    observations = centred(seeds[0], (SENSORS, HORIZON_LENGTH), 1.0, 6.0, ((0, 8), (1, 16)))
    loadings = centred(seeds[1], (SENSORS, FACTORS), 1.0, 6.0, ((0, 8),), jnp.float32)
    noise_var = jnp.clip(jnp.exp(math.log(4.0) - 2.7725887 * jax.random.uniform(seeds[2], (SENSORS,), jnp.float32) ** steps_of(seeds[2], (SENSORS,), ((0, 8),), -0.2, 0.2)), 0.25, 4.0)
    decay = draw_decay(jax.random.fold_in(seeds[5], 71), 0)
    tiles = draw_tiles(jax.random.fold_in(seeds[5], 71), 0)
    return {"observations": observations, "loadings": loadings, "noise_var": noise_var, "decay": decay, "tiles": tiles}


HIGH = lax.Precision.HIGHEST

def compose(before_seg, after_seg):
    return (before_seg[0] * after_seg[0], after_seg[0] * before_seg[1] + after_seg[1])

def reference(observations, loadings, noise_var, decay, tiles):
    block_hit = (tiles[:, 0][:, None] == jnp.arange(BLOCKS)[None, :]).astype(jnp.float32)
    window_hit = (tiles[:, 1][:, None] == jnp.arange(WINDOWS)[None, :]).astype(jnp.float32)
    tile_mask = jnp.dot(block_hit.T, window_hit, precision=HIGH)
    counts = jnp.sum(tile_mask, axis=1)
    windowed = observations.reshape(SENSORS, WINDOWS, WINDOW)

    def window_terms(index):
        sensor_mask = jnp.repeat(lax.dynamic_index_in_dim(tile_mask, index, 1, keepdims=False), BLOCK)
        weighted = loadings / noise_var[:, None] * sensor_mask[:, None]
        scaled = weighted.astype(jnp.bfloat16)
        obs_window = lax.dynamic_index_in_dim(windowed, index, 1, keepdims=False)
        info_vec = lax.dot_general(obs_window.astype(jnp.float32), scaled.astype(jnp.float32), (((0,), (0,)), ((), ())), preferred_element_type=jnp.float32)
        information = jnp.dot(weighted.T, loadings, precision=HIGH)
        return (info_vec, information)
    info_all, information_all = lax.map(window_terms, jnp.arange(WINDOWS))
    identity = jnp.eye(FACTORS, dtype=jnp.float32)
    covariance = jnp.linalg.solve(identity[None] + information_all, jnp.broadcast_to(identity, information_all.shape))
    local_est = jnp.einsum('wtk,wkj->wtj', info_all, covariance, precision=HIGH).reshape(HORIZON_LENGTH, FACTORS)
    forward = lax.associative_scan(compose, (decay, local_est), axis=0)[1]
    backward = jnp.flip(lax.associative_scan(compose, (jnp.flip(decay, 0), jnp.flip(local_est, 0)), axis=0)[1], 0)
    smoothed = ((1.0 - decay) / (1.0 + decay) * (forward + backward - local_est)).astype(jnp.bfloat16)
    smooth_win = smoothed.reshape(WINDOWS, WINDOW, FACTORS)
    smooth_wide = smooth_win.astype(jnp.float32)
    moments = jnp.einsum('wtk,wtj->wkj', smooth_wide, smooth_wide, precision=HIGH) + WINDOW * covariance

    def window_cross(totals, index):
        sensor_mask = jnp.repeat(lax.dynamic_index_in_dim(tile_mask, index, 1, keepdims=False), BLOCK)
        obs_window = lax.dynamic_index_in_dim(windowed, index, 1, keepdims=False)
        observed = obs_window * sensor_mask.astype(jnp.bfloat16)[:, None]
        smooth_now = lax.dynamic_index_in_dim(smooth_win, index, 0, keepdims=False)
        cross_terms = totals[0] + jnp.dot(observed.astype(jnp.float32), smooth_now.astype(jnp.float32), preferred_element_type=jnp.float32)
        sums_sq = totals[1] + jnp.sum(jnp.square(observed.astype(jnp.float32)), axis=1)
        return ((cross_terms, sums_sq), None)
    start_totals = (jnp.zeros((SENSORS, FACTORS), jnp.float32), jnp.zeros((SENSORS,), jnp.float32))
    (cross_terms, sums_sq), _ = lax.scan(window_cross, start_totals, jnp.arange(WINDOWS))
    block_moment = jnp.einsum('bw,wij->bij', tile_mask, moments, precision=HIGH)
    cross_blocks = cross_terms.reshape(BLOCKS, BLOCK, FACTORS)
    solved = jnp.linalg.solve(block_moment, jnp.swapaxes(cross_blocks, 1, 2))
    new_loadings = jnp.swapaxes(solved, 1, 2).reshape(SENSORS, FACTORS)
    explained = jnp.sum(new_loadings * cross_terms, axis=1)
    new_noise = (sums_sq - explained) / (WINDOW * jnp.repeat(counts, BLOCK))
    return (new_loadings, new_noise)
```

```python
import jax
import jax.numpy as jnp
from jax import lax
from jax.sharding import PartitionSpec as P

BLOCK = 128


HIGH = lax.Precision.HIGHEST


def compose(before_seg, after_seg):
    return (before_seg[0] * after_seg[0], after_seg[0] * before_seg[1] + after_seg[1])


def entering(gains, values, position):
    inclusive = lax.associative_scan(compose, (gains, values), axis=0)
    shifted_value = jnp.concatenate([jnp.zeros_like(values[:1]), inclusive[1][:-1]], 0)
    return lax.dynamic_index_in_dim(shifted_value, position, 0, keepdims=True)


def per_device(observations, loadings, noise_var, decay, tiles):
    sens_count = lax.axis_size("sens")
    time_count = lax.axis_size("tm")
    sens_index = lax.axis_index("sens")
    time_index = lax.axis_index("tm")
    sens_dev, window_len = observations.shape
    factors = loadings.shape[1]
    blocks_dev = sens_dev // BLOCK
    blocks_share = blocks_dev // time_count
    block_ids = sens_index * blocks_dev + jnp.arange(blocks_dev)
    block_hit = (tiles[:, 0][:, None] == block_ids[None, :]).astype(jnp.float32)
    window_hit = (tiles[:, 1][:, None] == jnp.arange(time_count)[None, :]).astype(jnp.float32)
    tile_mask = jnp.dot(block_hit.T, window_hit, precision=HIGH)
    present = lax.dynamic_index_in_dim(tile_mask, time_index, 1, keepdims=False)
    sensor_mask = jnp.repeat(present, BLOCK)
    weighted = loadings / noise_var[:, None] * sensor_mask[:, None]
    scaled = weighted.astype(jnp.bfloat16)
    info_part = lax.dot_general(
        observations, scaled, (((0,), (0,)), ((), ())), preferred_element_type=jnp.float32
    )
    gram_part = lax.dot_general(
        weighted, loadings, (((0,), (0,)), ((), ())), precision=lax.Precision.HIGH,
        preferred_element_type=jnp.float32,
    )
    summed = lax.psum(jnp.concatenate([info_part, gram_part], 0), "sens")
    info_vec = summed[:window_len]
    information = summed[window_len:]
    identity = jnp.eye(factors, dtype=jnp.float32)
    lower = jnp.linalg.cholesky(identity + information)
    covariance = jax.scipy.linalg.cho_solve((lower, True), identity)
    local_est = jnp.dot(info_vec, covariance, precision=HIGH)
    fwd_gain, fwd_local = lax.associative_scan(compose, (decay, local_est), axis=0)
    back_gain, back_local = lax.associative_scan(
        compose, (jnp.flip(decay, 0), jnp.flip(local_est, 0)), axis=0
    )
    summary = jnp.concatenate(
        [fwd_gain[-1:], fwd_local[-1:], back_gain[-1:], back_local[-1:]], 0
    )
    windows = lax.all_gather(summary, "tm", axis=0, tiled=False)
    enter_fwd = entering(windows[:, 0], windows[:, 1], time_index)
    enter_back = entering(
        jnp.flip(windows[:, 2], 0), jnp.flip(windows[:, 3], 0), time_count - 1 - time_index
    )
    back_gain = jnp.flip(back_gain, 0)
    back_local = jnp.flip(back_local, 0)
    forward = fwd_local + fwd_gain * enter_fwd
    backward = back_local + back_gain * enter_back
    smoothed = ((1.0 - decay) / (1.0 + decay) * (forward + backward - local_est)).astype(
        jnp.bfloat16
    )
    mask_mine = lax.dynamic_slice_in_dim(tile_mask, time_index * blocks_share, blocks_share, 0)
    observed = observations * sensor_mask.astype(jnp.bfloat16)[:, None]
    sums_sq = jnp.sum(jnp.square(observed.astype(jnp.float32)), axis=1)
    cross_terms = jnp.dot(observed, smoothed, preferred_element_type=jnp.float32)
    squares = lax.dot_general(
        smoothed, smoothed, (((0,), (0,)), ((), ())), preferred_element_type=jnp.float32
    )
    moment = squares + window_len * covariance
    share = sens_dev // time_count
    cross_mine = lax.psum_scatter(cross_terms, "tm", scatter_dimension=0, tiled=True)
    sq_mine = lax.psum_scatter(
        sums_sq.reshape(-1, factors), "tm", scatter_dimension=0, tiled=True
    ).reshape(share)
    all_moments = lax.all_gather(moment, "tm", axis=0, tiled=False)
    moment_mine = jnp.einsum("bw,wij->bij", mask_mine, all_moments, precision=HIGH)
    counts_mine = jnp.sum(mask_mine, axis=1)
    cross_blocks = cross_mine.reshape(blocks_share, BLOCK, factors)

    def solve_block(moment_block, cross_block):
        lower_block = jnp.linalg.cholesky(moment_block)
        return jax.scipy.linalg.cho_solve((lower_block, True), cross_block.T).T

    new_loadings = jax.vmap(solve_block)(moment_mine, cross_blocks).reshape(
        blocks_share * BLOCK, factors
    )
    explained = jnp.sum(new_loadings * cross_mine, axis=1)
    new_noise = (sq_mine - explained) / (window_len * jnp.repeat(counts_mine, BLOCK))
    return (new_loadings, new_noise)


def solution(mesh):
    return jax.shard_map(
        per_device,
        mesh=mesh,
        in_specs=(P("sens", "tm"), P("sens", None), P("sens"), P("tm", None), P()),
        out_specs=(P(("sens", "tm"), None), P(("sens", "tm"))),
        check_vma=False,
    )
```

```python
import jax
import jax.numpy as jnp
from jax import lax
from jax.experimental import pallas as pl
from jax.experimental.pallas import tpu as pltpu
from jax.sharding import PartitionSpec as P

BLOCK = 128


HIGH = lax.Precision.HIGHEST


def compose(before_seg, after_seg):
    return (before_seg[0] * after_seg[0], after_seg[0] * before_seg[1] + after_seg[1])


def _gauss_jordan(a_ref, o_ref):
    n = a_ref.shape[-1]
    o_ref[...] = a_ref[...]
    lane = lax.broadcasted_iota(jnp.int32, (1, 1, n), 2)
    sub = lax.broadcasted_iota(jnp.int32, (1, n, 1), 1)

    def step(k, carry):
        a = o_ref[...]
        colmask = lane == k
        rowmask = sub == k
        c = jnp.sum(jnp.where(colmask, a, 0.0), axis=2, keepdims=True)
        r = jnp.sum(jnp.where(rowmask, a, 0.0), axis=1, keepdims=True)
        p = jnp.sum(jnp.where(colmask, r, 0.0), axis=2, keepdims=True)
        inv_p = 1.0 / p
        rs = jnp.where(colmask, inv_p, r * inv_p)
        out = jnp.where(colmask, -c * inv_p, a - c * rs)
        o_ref[...] = jnp.where(rowmask, rs, out)
        return carry

    lax.fori_loop(0, n, step, 0)


def spd_inverse(a):
    return pl.pallas_call(
        _gauss_jordan,
        out_shape=jax.ShapeDtypeStruct(a.shape, jnp.float32),
        in_specs=[pl.BlockSpec(memory_space=pltpu.VMEM)],
        out_specs=pl.BlockSpec(memory_space=pltpu.VMEM),
    )(a)


def entering(gains, values, position):
    inclusive = lax.associative_scan(compose, (gains, values), axis=0)
    shifted_value = jnp.concatenate([jnp.zeros_like(values[:1]), inclusive[1][:-1]], 0)
    return lax.dynamic_index_in_dim(shifted_value, position, 0, keepdims=True)


def per_device(observations, loadings, noise_var, decay, tiles):
    sens_count = lax.axis_size("sens")
    time_count = lax.axis_size("tm")
    sens_index = lax.axis_index("sens")
    time_index = lax.axis_index("tm")
    sens_dev, window_len = observations.shape
    factors = loadings.shape[1]
    blocks_dev = sens_dev // BLOCK
    blocks_share = blocks_dev // time_count
    block_ids = sens_index * blocks_dev + jnp.arange(blocks_dev)
    block_hit = (tiles[:, 0][:, None] == block_ids[None, :]).astype(jnp.float32)
    window_hit = (tiles[:, 1][:, None] == jnp.arange(time_count)[None, :]).astype(jnp.float32)
    tile_mask = jnp.dot(block_hit.T, window_hit, precision=HIGH)
    present = lax.dynamic_index_in_dim(tile_mask, time_index, 1, keepdims=False)
    sensor_mask = jnp.repeat(present, BLOCK)
    weighted = loadings / noise_var[:, None] * sensor_mask[:, None]
    scaled = weighted.astype(jnp.bfloat16)
    info_part = lax.dot_general(
        observations, scaled, (((0,), (0,)), ((), ())), preferred_element_type=jnp.float32
    )
    weighted_lo = (weighted - scaled.astype(jnp.float32)).astype(jnp.bfloat16)
    loadings_hi = loadings.astype(jnp.bfloat16)
    loadings_lo = (loadings - loadings_hi.astype(jnp.float32)).astype(jnp.bfloat16)
    split = lax.dot_general(
        jnp.concatenate([scaled, weighted_lo], 1),
        jnp.concatenate([loadings_hi, loadings_lo], 1),
        (((0,), (0,)), ((), ())),
        preferred_element_type=jnp.float32,
    )
    gram_part = (
        split[:factors, :factors] + split[:factors, factors:] + split[factors:, :factors]
    )
    summed = lax.psum(jnp.concatenate([info_part, gram_part], 0), "sens")
    info_vec = summed[:window_len]
    information = summed[window_len:]
    identity = jnp.eye(factors, dtype=jnp.float32)
    covariance = spd_inverse((identity + information)[None])[0]
    local_est = jnp.dot(info_vec, covariance, precision=HIGH)
    fwd_gain, fwd_local = lax.associative_scan(compose, (decay, local_est), axis=0)
    back_gain, back_local = lax.associative_scan(
        compose, (jnp.flip(decay, 0), jnp.flip(local_est, 0)), axis=0
    )
    summary = jnp.concatenate(
        [fwd_gain[-1:], fwd_local[-1:], back_gain[-1:], back_local[-1:]], 0
    )
    windows = lax.all_gather(summary, "tm", axis=0, tiled=False)
    enter_fwd = entering(windows[:, 0], windows[:, 1], time_index)
    enter_back = entering(
        jnp.flip(windows[:, 2], 0), jnp.flip(windows[:, 3], 0), time_count - 1 - time_index
    )
    back_gain = jnp.flip(back_gain, 0)
    back_local = jnp.flip(back_local, 0)
    forward = fwd_local + fwd_gain * enter_fwd
    backward = back_local + back_gain * enter_back
    smoothed = ((1.0 - decay) / (1.0 + decay) * (forward + backward - local_est)).astype(
        jnp.bfloat16
    )
    mask_mine = lax.dynamic_slice_in_dim(tile_mask, time_index * blocks_share, blocks_share, 0)
    observed = observations * sensor_mask.astype(jnp.bfloat16)[:, None]
    sums_sq = jnp.sum(jnp.square(observed.astype(jnp.float32)), axis=1)
    cross_terms = jnp.dot(observed, smoothed, preferred_element_type=jnp.float32)
    squares = lax.dot_general(
        smoothed, smoothed, (((0,), (0,)), ((), ())), preferred_element_type=jnp.float32
    )
    moment = squares + window_len * covariance
    share = sens_dev // time_count
    cross_mine = lax.psum_scatter(cross_terms, "tm", scatter_dimension=0, tiled=True)
    sq_mine = lax.psum_scatter(
        sums_sq.reshape(-1, factors), "tm", scatter_dimension=0, tiled=True
    ).reshape(share)
    all_moments = lax.all_gather(moment, "tm", axis=0, tiled=False)
    moment_mine = jnp.einsum("bw,wij->bij", mask_mine, all_moments, precision=HIGH)
    counts_mine = jnp.sum(mask_mine, axis=1)
    cross_blocks = cross_mine.reshape(blocks_share, BLOCK, factors)
    inverse_mine = spd_inverse(moment_mine)
    new_loadings = jnp.einsum(
        "bsk,bjk->bsj", cross_blocks, inverse_mine, precision=HIGH
    ).reshape(blocks_share * BLOCK, factors)
    explained = jnp.sum(new_loadings * cross_mine, axis=1)
    new_noise = (sq_mine - explained) / (window_len * jnp.repeat(counts_mine, BLOCK))
    return (new_loadings, new_noise)


def solution(mesh):
    return jax.shard_map(
        per_device,
        mesh=mesh,
        in_specs=(P("sens", "tm"), P("sens", None), P("sens"), P("tm", None), P()),
        out_specs=(P(("sens", "tm"), None), P(("sens", "tm"))),
        check_vma=False,
    )
```

```python
import jax
import jax.numpy as jnp
from jax import lax
from jax.experimental import pallas as pl
from jax.experimental.pallas import tpu as pltpu
from jax.sharding import PartitionSpec as P

BLOCK = 128


HIGH = lax.Precision.HIGHEST


def compose(before_seg, after_seg):
    return (before_seg[0] * after_seg[0], after_seg[0] * before_seg[1] + after_seg[1])


def _gauss_jordan(a_ref, o_ref):
    n = a_ref.shape[-1]
    o_ref[...] = a_ref[...]
    lane = lax.broadcasted_iota(jnp.int32, (1, 1, n), 2)
    sub = lax.broadcasted_iota(jnp.int32, (1, n, 1), 1)

    def step(k, carry):
        a = o_ref[...]
        colmask = lane == k
        rowmask = sub == k
        c = jnp.sum(jnp.where(colmask, a, 0.0), axis=2, keepdims=True)
        r = jnp.sum(jnp.where(rowmask, a, 0.0), axis=1, keepdims=True)
        p = jnp.sum(jnp.where(colmask, r, 0.0), axis=2, keepdims=True)
        inv_p = 1.0 / p
        rs = jnp.where(colmask, inv_p, r * inv_p)
        out = jnp.where(colmask, -c * inv_p, a - c * rs)
        o_ref[...] = jnp.where(rowmask, rs, out)
        return carry

    lax.fori_loop(0, n, step, 0)


def spd_inverse(a):
    return pl.pallas_call(
        _gauss_jordan,
        out_shape=jax.ShapeDtypeStruct(a.shape, jnp.float32),
        in_specs=[pl.BlockSpec(memory_space=pltpu.VMEM)],
        out_specs=pl.BlockSpec(memory_space=pltpu.VMEM),
    )(a)


def entering(gains, values, position):
    inclusive = lax.associative_scan(compose, (gains, values), axis=0)
    shifted_value = jnp.concatenate([jnp.zeros_like(values[:1]), inclusive[1][:-1]], 0)
    return lax.dynamic_index_in_dim(shifted_value, position, 0, keepdims=True)


def per_device(observations, loadings, noise_var, decay, tiles):
    sens_count = lax.axis_size("sens")
    time_count = lax.axis_size("tm")
    sens_index = lax.axis_index("sens")
    time_index = lax.axis_index("tm")
    sens_dev, window_len = observations.shape
    factors = loadings.shape[1]
    blocks_dev = sens_dev // BLOCK
    blocks_share = blocks_dev // time_count
    block_ids = sens_index * blocks_dev + jnp.arange(blocks_dev)
    block_hit = (tiles[:, 0][:, None] == block_ids[None, :]).astype(jnp.float32)
    window_hit = (tiles[:, 1][:, None] == jnp.arange(time_count)[None, :]).astype(jnp.float32)
    tile_mask = jnp.dot(block_hit.T, window_hit, precision=HIGH)
    present = lax.dynamic_index_in_dim(tile_mask, time_index, 1, keepdims=False)
    sensor_mask = jnp.repeat(present, BLOCK)
    obs_mine = lax.all_to_all(observations, "tm", 0, 1, tiled=True)
    weighted = loadings / noise_var[:, None] * sensor_mask[:, None]
    scaled = weighted.astype(jnp.bfloat16)
    info_part = lax.dot_general(
        observations, scaled, (((0,), (0,)), ((), ())), preferred_element_type=jnp.float32
    )
    weighted_lo = (weighted - scaled.astype(jnp.float32)).astype(jnp.bfloat16)
    loadings_hi = loadings.astype(jnp.bfloat16)
    loadings_lo = (loadings - loadings_hi.astype(jnp.float32)).astype(jnp.bfloat16)
    split = lax.dot_general(
        jnp.concatenate([scaled, weighted_lo], 1),
        jnp.concatenate([loadings_hi, loadings_lo], 1),
        (((0,), (0,)), ((), ())),
        preferred_element_type=jnp.float32,
    )
    gram_part = (
        split[:factors, :factors] + split[:factors, factors:] + split[factors:, :factors]
    )
    summed = lax.psum(jnp.concatenate([info_part, gram_part], 0), "sens")
    info_vec = summed[:window_len]
    information = summed[window_len:]
    identity = jnp.eye(factors, dtype=jnp.float32)
    covariance = spd_inverse((identity + information)[None])[0]
    local_est = jnp.dot(info_vec, covariance, precision=HIGH)
    fwd_gain, fwd_local = lax.associative_scan(compose, (decay, local_est), axis=0)
    back_gain, back_local = lax.associative_scan(
        compose, (jnp.flip(decay, 0), jnp.flip(local_est, 0)), axis=0
    )
    summary = jnp.concatenate(
        [fwd_gain[-1:], fwd_local[-1:], back_gain[-1:], back_local[-1:]], 0
    )
    windows = lax.all_gather(summary, "tm", axis=0, tiled=False)
    enter_fwd = entering(windows[:, 0], windows[:, 1], time_index)
    enter_back = entering(
        jnp.flip(windows[:, 2], 0), jnp.flip(windows[:, 3], 0), time_count - 1 - time_index
    )
    back_gain = jnp.flip(back_gain, 0)
    back_local = jnp.flip(back_local, 0)
    forward = fwd_local + fwd_gain * enter_fwd
    backward = back_local + back_gain * enter_back
    smoothed = ((1.0 - decay) / (1.0 + decay) * (forward + backward - local_est)).astype(
        jnp.bfloat16
    )
    mask_mine = lax.dynamic_slice_in_dim(tile_mask, time_index * blocks_share, blocks_share, 0)
    squares = lax.dot_general(
        smoothed, smoothed, (((0,), (0,)), ((), ())), preferred_element_type=jnp.float32
    )
    moment = squares + window_len * covariance
    gathered = lax.all_gather(
        jnp.concatenate([smoothed.astype(jnp.float32), moment], 0), "tm", axis=0, tiled=False
    )
    smooth_all = gathered[:, :window_len].reshape(time_count * window_len, factors)
    all_moments = gathered[:, window_len:]
    mask_full = jnp.broadcast_to(
        mask_mine[:, None, :, None], (blocks_share, BLOCK, time_count, window_len)
    ).reshape(blocks_share * BLOCK, time_count * window_len)
    observed = obs_mine * mask_full.astype(jnp.bfloat16)
    sq_mine = jnp.sum(jnp.square(observed.astype(jnp.float32)), axis=1)
    cross_mine = jnp.dot(
        observed, smooth_all.astype(jnp.bfloat16), preferred_element_type=jnp.float32
    )
    moment_mine = jnp.einsum("bw,wij->bij", mask_mine, all_moments, precision=HIGH)
    counts_mine = jnp.sum(mask_mine, axis=1)
    cross_blocks = cross_mine.reshape(blocks_share, BLOCK, factors)
    inverse_mine = spd_inverse(moment_mine)
    new_loadings = jnp.einsum(
        "bsk,bjk->bsj", cross_blocks, inverse_mine, precision=HIGH
    ).reshape(blocks_share * BLOCK, factors)
    explained = jnp.sum(new_loadings * cross_mine, axis=1)
    new_noise = (sq_mine - explained) / (window_len * jnp.repeat(counts_mine, BLOCK))
    return (new_loadings, new_noise)


def solution(mesh):
    return jax.shard_map(
        per_device,
        mesh=mesh,
        in_specs=(P("sens", "tm"), P("sens", None), P("sens"), P("tm", None), P()),
        out_specs=(P(("sens", "tm"), None), P(("sens", "tm"))),
        check_vma=False,
    )
```

```python
import jax
import jax.numpy as jnp
from jax import lax
from jax.experimental import pallas as pl
from jax.experimental.pallas import tpu as pltpu
from jax.sharding import PartitionSpec as P

BLOCK = 128


HIGH = lax.Precision.HIGHEST


def compose(before_seg, after_seg):
    return (before_seg[0] * after_seg[0], after_seg[0] * before_seg[1] + after_seg[1])


def _gauss_jordan(a_ref, o_ref):
    n = a_ref.shape[-1]
    o_ref[...] = a_ref[...]
    lane = lax.broadcasted_iota(jnp.int32, (1, 1, n), 2)
    sub = lax.broadcasted_iota(jnp.int32, (1, n, 1), 1)

    def step(k, carry):
        a = o_ref[...]
        colmask = lane == k
        rowmask = sub == k
        c = jnp.sum(jnp.where(colmask, a, 0.0), axis=2, keepdims=True)
        r = jnp.sum(jnp.where(rowmask, a, 0.0), axis=1, keepdims=True)
        p = jnp.sum(jnp.where(colmask, r, 0.0), axis=2, keepdims=True)
        inv_p = 1.0 / p
        rs = jnp.where(colmask, inv_p, r * inv_p)
        out = jnp.where(colmask, -c * inv_p, a - c * rs)
        o_ref[...] = jnp.where(rowmask, rs, out)
        return carry

    lax.fori_loop(0, n, step, 0)


def spd_inverse(a):
    return pl.pallas_call(
        _gauss_jordan,
        out_shape=jax.ShapeDtypeStruct(a.shape, jnp.float32),
        in_specs=[pl.BlockSpec(memory_space=pltpu.VMEM)],
        out_specs=pl.BlockSpec(memory_space=pltpu.VMEM),
    )(a)


def butterfly_sum(part, axis, count):
    distance = 1
    while distance < count:
        pairs = [(i, i ^ distance) for i in range(count)]
        part = part + lax.ppermute(part, axis, pairs)
        distance *= 2
    return part


def per_device(observations, loadings, noise_var, decay, tiles):
    sens_count = lax.axis_size("sens")
    time_count = lax.axis_size("tm")
    sens_index = lax.axis_index("sens")
    time_index = lax.axis_index("tm")
    sens_dev, window_len = observations.shape
    factors = loadings.shape[1]
    blocks_dev = sens_dev // BLOCK
    blocks_share = blocks_dev // time_count
    block_ids = sens_index * blocks_dev + jnp.arange(blocks_dev)
    block_hit = (tiles[:, 0][:, None] == block_ids[None, :]).astype(jnp.float32)
    window_hit = (tiles[:, 1][:, None] == jnp.arange(time_count)[None, :]).astype(jnp.float32)
    tile_mask = jnp.dot(block_hit.T, window_hit, precision=HIGH)
    present = lax.dynamic_index_in_dim(tile_mask, time_index, 1, keepdims=False)
    sensor_mask = jnp.repeat(present, BLOCK)
    obs_mine = lax.all_to_all(observations, "tm", 0, 1, tiled=True)
    weighted = loadings / noise_var[:, None] * sensor_mask[:, None]
    scaled = weighted.astype(jnp.bfloat16)
    info_part = lax.dot_general(
        observations, scaled, (((0,), (0,)), ((), ())), preferred_element_type=jnp.float32
    )
    weighted_lo = (weighted - scaled.astype(jnp.float32)).astype(jnp.bfloat16)
    loadings_hi = loadings.astype(jnp.bfloat16)
    loadings_lo = (loadings - loadings_hi.astype(jnp.float32)).astype(jnp.bfloat16)
    split = lax.dot_general(
        jnp.concatenate([scaled, weighted_lo], 1),
        jnp.concatenate([loadings_hi, loadings_lo], 1),
        (((0,), (0,)), ((), ())),
        preferred_element_type=jnp.float32,
    )
    gram_part = (
        split[:factors, :factors] + split[:factors, factors:] + split[factors:, :factors]
    )
    summed = butterfly_sum(jnp.concatenate([info_part, gram_part], 0), "sens", sens_count)
    info_vec = summed[:window_len]
    information = summed[window_len:]
    identity = jnp.eye(factors, dtype=jnp.float32)
    covariance = spd_inverse((identity + information)[None])[0]
    local_est = jnp.dot(info_vec, covariance, precision=HIGH)
    gathered = lax.all_gather(
        jnp.concatenate([local_est, decay, covariance], 0), "tm", axis=0, tiled=False
    )
    steps = time_count * window_len
    est_all = gathered[:, :window_len].reshape(steps, factors)
    decay_all = gathered[:, window_len : 2 * window_len].reshape(steps, factors)
    cov_all = gathered[:, 2 * window_len :]
    forward = lax.associative_scan(compose, (decay_all, est_all), axis=0)[1]
    backward = jnp.flip(
        lax.associative_scan(compose, (jnp.flip(decay_all, 0), jnp.flip(est_all, 0)), axis=0)[1],
        0,
    )
    smooth_all = (
        (1.0 - decay_all) / (1.0 + decay_all) * (forward + backward - est_all)
    ).astype(jnp.bfloat16)
    smooth_win = smooth_all.reshape(time_count, window_len, factors)
    all_moments = (
        jnp.einsum("wtk,wtj->wkj", smooth_win, smooth_win, preferred_element_type=jnp.float32)
        + window_len * cov_all
    )
    mask_mine = lax.dynamic_slice_in_dim(tile_mask, time_index * blocks_share, blocks_share, 0)
    mask_full = jnp.broadcast_to(
        mask_mine[:, None, :, None], (blocks_share, BLOCK, time_count, window_len)
    ).reshape(blocks_share * BLOCK, time_count * window_len)
    observed = obs_mine * mask_full.astype(jnp.bfloat16)
    sq_mine = jnp.sum(jnp.square(observed.astype(jnp.float32)), axis=1)
    cross_mine = jnp.dot(observed, smooth_all, preferred_element_type=jnp.float32)
    moment_mine = jnp.einsum("bw,wij->bij", mask_mine, all_moments, precision=HIGH)
    counts_mine = jnp.sum(mask_mine, axis=1)
    cross_blocks = cross_mine.reshape(blocks_share, BLOCK, factors)
    inverse_mine = spd_inverse(moment_mine)
    new_loadings = jnp.einsum(
        "bsk,bjk->bsj", cross_blocks, inverse_mine, precision=HIGH
    ).reshape(blocks_share * BLOCK, factors)
    explained = jnp.sum(new_loadings * cross_mine, axis=1)
    new_noise = (sq_mine - explained) / (window_len * jnp.repeat(counts_mine, BLOCK))
    return (new_loadings, new_noise)


def solution(mesh):
    return jax.shard_map(
        per_device,
        mesh=mesh,
        in_specs=(P("sens", "tm"), P("sens", None), P("sens"), P("tm", None), P()),
        out_specs=(P(("sens", "tm"), None), P(("sens", "tm"))),
        check_vma=False,
    )
```

```python
import jax
import jax.numpy as jnp
from jax import lax
from jax.experimental import pallas as pl
from jax.experimental.pallas import tpu as pltpu
from jax.sharding import PartitionSpec as P

BLOCK = 128


HIGH = lax.Precision.HIGHEST


def compose(before_seg, after_seg):
    return (before_seg[0] * after_seg[0], after_seg[0] * before_seg[1] + after_seg[1])


def _gauss_jordan(a_ref, o_ref):
    n = a_ref.shape[-1]
    o_ref[...] = a_ref[...]
    lane = lax.broadcasted_iota(jnp.int32, (1, 1, n), 2)
    sub = lax.broadcasted_iota(jnp.int32, (1, n, 1), 1)

    def step(k, carry):
        a = o_ref[...]
        colmask = lane == k
        rowmask = sub == k
        c = jnp.sum(jnp.where(colmask, a, 0.0), axis=2, keepdims=True)
        r = jnp.sum(jnp.where(rowmask, a, 0.0), axis=1, keepdims=True)
        p = jnp.sum(jnp.where(colmask, r, 0.0), axis=2, keepdims=True)
        inv_p = 1.0 / p
        rs = jnp.where(colmask, inv_p, r * inv_p)
        out = jnp.where(colmask, -c * inv_p, a - c * rs)
        o_ref[...] = jnp.where(rowmask, rs, out)
        return carry

    lax.fori_loop(0, n, step, 0)


def spd_inverse(a):
    return pl.pallas_call(
        _gauss_jordan,
        out_shape=jax.ShapeDtypeStruct(a.shape, jnp.float32),
        in_specs=[pl.BlockSpec(memory_space=pltpu.VMEM)],
        out_specs=pl.BlockSpec(memory_space=pltpu.VMEM),
    )(a)


def butterfly_sum(part, axis, count):
    distance = 1
    while distance < count:
        pairs = [(i, i ^ distance) for i in range(count)]
        part = part + lax.ppermute(part, axis, pairs)
        distance *= 2
    return part


def butterfly_gather(part, axis, count):
    place = lax.axis_index(axis)
    held = part[None]
    distance = 1
    while distance < count:
        pairs = [(i, i ^ distance) for i in range(count)]
        other = lax.ppermute(held, axis, pairs)
        upper = (place // distance) % 2 == 1
        held = jnp.where(
            upper, jnp.concatenate([other, held], 0), jnp.concatenate([held, other], 0)
        )
        distance *= 2
    return held


def entering(gains, values, position):
    inclusive = lax.associative_scan(compose, (gains, values), axis=0)
    shifted_value = jnp.concatenate([jnp.zeros_like(values[:1]), inclusive[1][:-1]], 0)
    return lax.dynamic_index_in_dim(shifted_value, position, 0, keepdims=True)


def per_device(observations, loadings, noise_var, decay, tiles):
    sens_count = lax.axis_size("sens")
    time_count = lax.axis_size("tm")
    sens_index = lax.axis_index("sens")
    time_index = lax.axis_index("tm")
    sens_dev, window_len = observations.shape
    factors = loadings.shape[1]
    blocks_dev = sens_dev // BLOCK
    blocks_share = blocks_dev // time_count
    block_ids = sens_index * blocks_dev + jnp.arange(blocks_dev)
    block_hit = (tiles[:, 0][:, None] == block_ids[None, :]).astype(jnp.float32)
    window_hit = (tiles[:, 1][:, None] == jnp.arange(time_count)[None, :]).astype(jnp.float32)
    tile_mask = jnp.dot(block_hit.T, window_hit, precision=HIGH)
    present = lax.dynamic_index_in_dim(tile_mask, time_index, 1, keepdims=False)
    sensor_mask = jnp.repeat(present, BLOCK)
    obs_mine = lax.all_to_all(observations, "tm", 0, 1, tiled=True)
    weighted = loadings / noise_var[:, None] * sensor_mask[:, None]
    scaled = weighted.astype(jnp.bfloat16)
    info_part = lax.dot_general(
        observations, scaled, (((0,), (0,)), ((), ())), preferred_element_type=jnp.float32
    )
    weighted_lo = (weighted - scaled.astype(jnp.float32)).astype(jnp.bfloat16)
    loadings_hi = loadings.astype(jnp.bfloat16)
    loadings_lo = (loadings - loadings_hi.astype(jnp.float32)).astype(jnp.bfloat16)
    split = lax.dot_general(
        jnp.concatenate([scaled, weighted_lo], 1),
        jnp.concatenate([loadings_hi, loadings_lo], 1),
        (((0,), (0,)), ((), ())),
        preferred_element_type=jnp.float32,
    )
    gram_part = (
        split[:factors, :factors] + split[:factors, factors:] + split[factors:, :factors]
    )
    summed = butterfly_sum(jnp.concatenate([info_part, gram_part], 0), "sens", sens_count)
    info_vec = summed[:window_len]
    information = summed[window_len:]
    identity = jnp.eye(factors, dtype=jnp.float32)
    covariance = spd_inverse((identity + information)[None])[0]
    local_est = jnp.dot(info_vec, covariance, precision=HIGH)
    fwd_gain, fwd_local = lax.associative_scan(compose, (decay, local_est), axis=0)
    back_gain, back_local = lax.associative_scan(
        compose, (jnp.flip(decay, 0), jnp.flip(local_est, 0)), axis=0
    )
    summary = jnp.concatenate(
        [fwd_gain[-1:], fwd_local[-1:], back_gain[-1:], back_local[-1:]], 0
    )
    windows = butterfly_gather(summary, "tm", time_count)
    enter_fwd = entering(windows[:, 0], windows[:, 1], time_index)
    enter_back = entering(
        jnp.flip(windows[:, 2], 0), jnp.flip(windows[:, 3], 0), time_count - 1 - time_index
    )
    back_gain = jnp.flip(back_gain, 0)
    back_local = jnp.flip(back_local, 0)
    forward = fwd_local + fwd_gain * enter_fwd
    backward = back_local + back_gain * enter_back
    smoothed = ((1.0 - decay) / (1.0 + decay) * (forward + backward - local_est)).astype(
        jnp.bfloat16
    )
    mask_mine = lax.dynamic_slice_in_dim(tile_mask, time_index * blocks_share, blocks_share, 0)
    squares = lax.dot_general(
        smoothed, smoothed, (((0,), (0,)), ((), ())), preferred_element_type=jnp.float32
    )
    moment = squares + window_len * covariance
    gathered = lax.all_gather(
        jnp.concatenate([smoothed.astype(jnp.float32), moment], 0), "tm", axis=0, tiled=False
    )
    smooth_all = gathered[:, :window_len].reshape(time_count * window_len, factors)
    all_moments = gathered[:, window_len:]
    mask_full = jnp.broadcast_to(
        mask_mine[:, None, :, None], (blocks_share, BLOCK, time_count, window_len)
    ).reshape(blocks_share * BLOCK, time_count * window_len)
    observed = obs_mine * mask_full.astype(jnp.bfloat16)
    sq_mine = jnp.sum(jnp.square(observed.astype(jnp.float32)), axis=1)
    cross_mine = jnp.dot(
        observed, smooth_all.astype(jnp.bfloat16), preferred_element_type=jnp.float32
    )
    moment_mine = jnp.einsum("bw,wij->bij", mask_mine, all_moments, precision=HIGH)
    counts_mine = jnp.sum(mask_mine, axis=1)
    cross_blocks = cross_mine.reshape(blocks_share, BLOCK, factors)
    inverse_mine = spd_inverse(moment_mine)
    new_loadings = jnp.einsum(
        "bsk,bjk->bsj", cross_blocks, inverse_mine, precision=HIGH
    ).reshape(blocks_share * BLOCK, factors)
    explained = jnp.sum(new_loadings * cross_mine, axis=1)
    new_noise = (sq_mine - explained) / (window_len * jnp.repeat(counts_mine, BLOCK))
    return (new_loadings, new_noise)


def solution(mesh):
    return jax.shard_map(
        per_device,
        mesh=mesh,
        in_specs=(P("sens", "tm"), P("sens", None), P("sens"), P("tm", None), P()),
        out_specs=(P(("sens", "tm"), None), P(("sens", "tm"))),
        check_vma=False,
    )
```

```python
import jax
import jax.numpy as jnp
from jax import lax
from jax.experimental import pallas as pl
from jax.experimental.pallas import tpu as pltpu
from jax.sharding import PartitionSpec as P

BLOCK = 128


HIGH = lax.Precision.HIGHEST


def compose(before_seg, after_seg):
    return (before_seg[0] * after_seg[0], after_seg[0] * before_seg[1] + after_seg[1])


def _gauss_jordan(a_ref, o_ref):
    n = a_ref.shape[-1]
    o_ref[...] = a_ref[...]
    lane = lax.broadcasted_iota(jnp.int32, (1, 1, n), 2)
    sub = lax.broadcasted_iota(jnp.int32, (1, n, 1), 1)

    def step(k, carry):
        a = o_ref[...]
        colmask = lane == k
        rowmask = sub == k
        c = jnp.sum(jnp.where(colmask, a, 0.0), axis=2, keepdims=True)
        r = jnp.sum(jnp.where(rowmask, a, 0.0), axis=1, keepdims=True)
        p = jnp.sum(jnp.where(colmask, r, 0.0), axis=2, keepdims=True)
        inv_p = 1.0 / p
        rs = jnp.where(colmask, inv_p, r * inv_p)
        out = jnp.where(colmask, -c * inv_p, a - c * rs)
        o_ref[...] = jnp.where(rowmask, rs, out)
        return carry

    lax.fori_loop(0, n, step, 0)


def spd_inverse(a):
    return pl.pallas_call(
        _gauss_jordan,
        out_shape=jax.ShapeDtypeStruct(a.shape, jnp.float32),
        in_specs=[pl.BlockSpec(memory_space=pltpu.VMEM)],
        out_specs=pl.BlockSpec(memory_space=pltpu.VMEM),
    )(a)


def butterfly_sum(part, axis, count):
    distance = 1
    while distance < count:
        pairs = [(i, i ^ distance) for i in range(count)]
        part = part + lax.ppermute(part, axis, pairs)
        distance *= 2
    return part


def butterfly_gather(part, axis, count):
    place = lax.axis_index(axis)
    held = part[None]
    distance = 1
    while distance < count:
        pairs = [(i, i ^ distance) for i in range(count)]
        other = lax.ppermute(held, axis, pairs)
        upper = (place // distance) % 2 == 1
        held = jnp.where(
            upper, jnp.concatenate([other, held], 0), jnp.concatenate([held, other], 0)
        )
        distance *= 2
    return held


def entering(gains, values, position):
    inclusive = lax.associative_scan(compose, (gains, values), axis=0)
    shifted_value = jnp.concatenate([jnp.zeros_like(values[:1]), inclusive[1][:-1]], 0)
    return lax.dynamic_index_in_dim(shifted_value, position, 0, keepdims=True)


def per_device(observations, loadings, noise_var, decay, tiles):
    sens_count = lax.axis_size("sens")
    time_count = lax.axis_size("tm")
    sens_index = lax.axis_index("sens")
    time_index = lax.axis_index("tm")
    sens_dev, window_len = observations.shape
    factors = loadings.shape[1]
    blocks_dev = sens_dev // BLOCK
    blocks_share = blocks_dev // time_count
    block_ids = sens_index * blocks_dev + jnp.arange(blocks_dev)
    block_hit = (tiles[:, 0][:, None] == block_ids[None, :]).astype(jnp.float32)
    window_hit = (tiles[:, 1][:, None] == jnp.arange(time_count)[None, :]).astype(jnp.float32)
    tile_mask = jnp.dot(block_hit.T, window_hit, precision=HIGH)
    present = lax.dynamic_index_in_dim(tile_mask, time_index, 1, keepdims=False)
    sensor_mask = jnp.repeat(present, BLOCK)
    obs_mine = lax.all_to_all(observations, "tm", 0, 1, tiled=True)
    weighted = loadings / noise_var[:, None] * sensor_mask[:, None]
    scaled = weighted.astype(jnp.bfloat16)
    info_part = lax.dot_general(
        observations, scaled, (((0,), (0,)), ((), ())), preferred_element_type=jnp.float32
    )
    weighted_lo = (weighted - scaled.astype(jnp.float32)).astype(jnp.bfloat16)
    loadings_hi = loadings.astype(jnp.bfloat16)
    loadings_lo = (loadings - loadings_hi.astype(jnp.float32)).astype(jnp.bfloat16)
    split = lax.dot_general(
        jnp.concatenate([scaled, weighted_lo], 1),
        jnp.concatenate([loadings_hi, loadings_lo], 1),
        (((0,), (0,)), ((), ())),
        preferred_element_type=jnp.float32,
    )
    gram_part = (
        split[:factors, :factors] + split[:factors, factors:] + split[factors:, :factors]
    )
    summed = butterfly_sum(jnp.concatenate([info_part, gram_part], 0), "sens", sens_count)
    info_vec = summed[:window_len]
    information = summed[window_len:]
    identity = jnp.eye(factors, dtype=jnp.float32)
    covariance = spd_inverse((identity + information)[None])[0]
    cov_all = lax.all_gather(covariance, "tm", axis=0, tiled=False)
    local_est = jnp.dot(info_vec, covariance, precision=HIGH)
    fwd_gain, fwd_local = lax.associative_scan(compose, (decay, local_est), axis=0)
    back_gain, back_local = lax.associative_scan(
        compose, (jnp.flip(decay, 0), jnp.flip(local_est, 0)), axis=0
    )
    summary = jnp.concatenate(
        [fwd_gain[-1:], fwd_local[-1:], back_gain[-1:], back_local[-1:]], 0
    )
    windows = butterfly_gather(summary, "tm", time_count)
    enter_fwd = entering(windows[:, 0], windows[:, 1], time_index)
    enter_back = entering(
        jnp.flip(windows[:, 2], 0), jnp.flip(windows[:, 3], 0), time_count - 1 - time_index
    )
    back_gain = jnp.flip(back_gain, 0)
    back_local = jnp.flip(back_local, 0)
    forward = fwd_local + fwd_gain * enter_fwd
    backward = back_local + back_gain * enter_back
    smoothed = ((1.0 - decay) / (1.0 + decay) * (forward + backward - local_est)).astype(
        jnp.bfloat16
    )
    mask_mine = lax.dynamic_slice_in_dim(tile_mask, time_index * blocks_share, blocks_share, 0)
    smooth_win = lax.all_gather(smoothed, "tm", axis=0, tiled=False)
    smooth_all = smooth_win.reshape(time_count * window_len, factors)
    all_moments = (
        jnp.einsum("wtk,wtj->wkj", smooth_win, smooth_win, preferred_element_type=jnp.float32)
        + window_len * cov_all
    )
    mask_full = jnp.broadcast_to(
        mask_mine[:, None, :, None], (blocks_share, BLOCK, time_count, window_len)
    ).reshape(blocks_share * BLOCK, time_count * window_len)
    observed = obs_mine * mask_full.astype(jnp.bfloat16)
    sq_mine = jnp.sum(jnp.square(observed.astype(jnp.float32)), axis=1)
    cross_mine = jnp.dot(observed, smooth_all, preferred_element_type=jnp.float32)
    moment_mine = jnp.einsum("bw,wij->bij", mask_mine, all_moments, precision=HIGH)
    counts_mine = jnp.sum(mask_mine, axis=1)
    cross_blocks = cross_mine.reshape(blocks_share, BLOCK, factors)
    inverse_mine = spd_inverse(moment_mine)
    new_loadings = jnp.einsum(
        "bsk,bjk->bsj", cross_blocks, inverse_mine, precision=HIGH
    ).reshape(blocks_share * BLOCK, factors)
    explained = jnp.sum(new_loadings * cross_mine, axis=1)
    new_noise = (sq_mine - explained) / (window_len * jnp.repeat(counts_mine, BLOCK))
    return (new_loadings, new_noise)


def solution(mesh):
    return jax.shard_map(
        per_device,
        mesh=mesh,
        in_specs=(P("sens", "tm"), P("sens", None), P("sens"), P("tm", None), P()),
        out_specs=(P(("sens", "tm"), None), P(("sens", "tm"))),
        check_vma=False,
    )
```

```python
import jax
import jax.numpy as jnp
from jax import lax
from jax.experimental import pallas as pl
from jax.experimental.pallas import tpu as pltpu
from jax.sharding import PartitionSpec as P

BLOCK = 128


HIGH = lax.Precision.HIGHEST


def compose(before_seg, after_seg):
    return (before_seg[0] * after_seg[0], after_seg[0] * before_seg[1] + after_seg[1])


def _gauss_jordan(a_ref, o_ref):
    n = a_ref.shape[-1]
    o_ref[...] = a_ref[...]
    lane = lax.broadcasted_iota(jnp.int32, (1, 1, n), 2)
    sub = lax.broadcasted_iota(jnp.int32, (1, n, 1), 1)

    def step(k, carry):
        a = o_ref[...]
        colmask = lane == k
        rowmask = sub == k
        c = jnp.sum(jnp.where(colmask, a, 0.0), axis=2, keepdims=True)
        r = jnp.sum(jnp.where(rowmask, a, 0.0), axis=1, keepdims=True)
        p = jnp.sum(jnp.where(colmask, r, 0.0), axis=2, keepdims=True)
        inv_p = 1.0 / p
        rs = jnp.where(colmask, inv_p, r * inv_p)
        out = jnp.where(colmask, -c * inv_p, a - c * rs)
        o_ref[...] = jnp.where(rowmask, rs, out)
        return carry

    lax.fori_loop(0, n, step, 0)


def spd_inverse(a):
    batch, n, _ = a.shape
    return pl.pallas_call(
        _gauss_jordan,
        out_shape=jax.ShapeDtypeStruct(a.shape, jnp.float32),
        in_specs=[pl.BlockSpec(memory_space=pltpu.VMEM)],
        out_specs=pl.BlockSpec(memory_space=pltpu.VMEM),
        cost_estimate=pl.CostEstimate(
            flops=8 * batch * n * n * n, transcendentals=0, bytes_accessed=8 * batch * n * n
        ),
    )(a)


def butterfly_sum(part, axis, count):
    distance = 1
    while distance < count:
        pairs = [(i, i ^ distance) for i in range(count)]
        part = part + lax.ppermute(part, axis, pairs)
        distance *= 2
    return part


def butterfly_gather(part, axis, count):
    place = lax.axis_index(axis)
    held = part[None]
    distance = 1
    while distance < count:
        pairs = [(i, i ^ distance) for i in range(count)]
        other = lax.ppermute(held, axis, pairs)
        upper = (place // distance) % 2 == 1
        held = jnp.where(
            upper, jnp.concatenate([other, held], 0), jnp.concatenate([held, other], 0)
        )
        distance *= 2
    return held


def entering(gains, values, position):
    inclusive = lax.associative_scan(compose, (gains, values), axis=0)
    shifted_value = jnp.concatenate([jnp.zeros_like(values[:1]), inclusive[1][:-1]], 0)
    return lax.dynamic_index_in_dim(shifted_value, position, 0, keepdims=True)


def per_device(observations, loadings, noise_var, decay, tiles):
    sens_count = lax.axis_size("sens")
    time_count = lax.axis_size("tm")
    sens_index = lax.axis_index("sens")
    time_index = lax.axis_index("tm")
    sens_dev, window_len = observations.shape
    factors = loadings.shape[1]
    blocks_dev = sens_dev // BLOCK
    blocks_share = blocks_dev // time_count
    block_ids = sens_index * blocks_dev + jnp.arange(blocks_dev)
    block_hit = (tiles[:, 0][:, None] == block_ids[None, :]).astype(jnp.float32)
    window_hit = (tiles[:, 1][:, None] == jnp.arange(time_count)[None, :]).astype(jnp.float32)
    tile_mask = jnp.dot(block_hit.T, window_hit, precision=HIGH)
    present = lax.dynamic_index_in_dim(tile_mask, time_index, 1, keepdims=False)
    sensor_mask = jnp.repeat(present, BLOCK)
    obs_mine = lax.all_to_all(observations, "tm", 0, 1, tiled=True)
    weighted = loadings * (1.0 / noise_var)[:, None] * sensor_mask[:, None]
    scaled = weighted.astype(jnp.bfloat16)
    weighted_lo = (weighted - scaled.astype(jnp.float32)).astype(jnp.bfloat16)
    loadings_hi = loadings.astype(jnp.bfloat16)
    loadings_lo = (loadings - loadings_hi.astype(jnp.float32)).astype(jnp.bfloat16)
    split = lax.dot_general(
        jnp.concatenate([scaled, weighted_lo], 1),
        jnp.concatenate([loadings_hi, loadings_lo], 1),
        (((0,), (0,)), ((), ())),
        preferred_element_type=jnp.float32,
    )
    gram_part = (
        split[:factors, :factors] + split[:factors, factors:] + split[factors:, :factors]
    )
    information = butterfly_sum(gram_part, "sens", sens_count)
    info_part = lax.dot_general(
        observations, scaled, (((0,), (0,)), ((), ())), preferred_element_type=jnp.float32
    )
    info_vec = butterfly_sum(info_part, "sens", sens_count)
    identity = jnp.eye(factors, dtype=jnp.float32)
    covariance = spd_inverse((identity + information)[None])[0]
    local_est = jnp.dot(info_vec, covariance, precision=HIGH)
    fwd_gain, fwd_local = lax.associative_scan(compose, (decay, local_est), axis=0)
    back_gain, back_local = lax.associative_scan(
        compose, (jnp.flip(decay, 0), jnp.flip(local_est, 0)), axis=0
    )
    summary = jnp.concatenate(
        [fwd_gain[-1:], fwd_local[-1:], back_gain[-1:], back_local[-1:]], 0
    )
    windows = butterfly_gather(summary, "tm", time_count)
    enter_fwd = entering(windows[:, 0], windows[:, 1], time_index)
    enter_back = entering(
        jnp.flip(windows[:, 2], 0), jnp.flip(windows[:, 3], 0), time_count - 1 - time_index
    )
    back_gain = jnp.flip(back_gain, 0)
    back_local = jnp.flip(back_local, 0)
    forward = fwd_local + fwd_gain * enter_fwd
    backward = back_local + back_gain * enter_back
    smoothed = ((1.0 - decay) / (1.0 + decay) * (forward + backward - local_est)).astype(
        jnp.bfloat16
    )
    mask_mine = lax.dynamic_slice_in_dim(tile_mask, time_index * blocks_share, blocks_share, 0)
    squares = lax.dot_general(
        smoothed, smoothed, (((0,), (0,)), ((), ())), preferred_element_type=jnp.float32
    )
    moment = squares + window_len * covariance
    gathered = lax.all_gather(
        jnp.concatenate([smoothed.astype(jnp.float32), moment], 0), "tm", axis=0, tiled=False
    )
    smooth_all = gathered[:, :window_len].reshape(time_count * window_len, factors)
    all_moments = gathered[:, window_len:]
    mask_full = jnp.broadcast_to(
        mask_mine[:, None, :, None], (blocks_share, BLOCK, time_count, window_len)
    ).reshape(blocks_share * BLOCK, time_count * window_len)
    observed = obs_mine * mask_full.astype(jnp.bfloat16)
    sq_mine = jnp.sum(jnp.square(observed.astype(jnp.float32)), axis=1)
    cross_mine = jnp.dot(
        observed, smooth_all.astype(jnp.bfloat16), preferred_element_type=jnp.float32
    )
    moment_mine = jnp.einsum("bw,wij->bij", mask_mine, all_moments, precision=HIGH)
    counts_mine = jnp.sum(mask_mine, axis=1)
    cross_blocks = cross_mine.reshape(blocks_share, BLOCK, factors)
    inverse_mine = spd_inverse(moment_mine)
    new_loadings = jnp.einsum(
        "bsk,bjk->bsj", cross_blocks, inverse_mine, precision=HIGH
    ).reshape(blocks_share * BLOCK, factors)
    explained = jnp.sum(new_loadings * cross_mine, axis=1)
    new_noise = (sq_mine - explained) / (window_len * jnp.repeat(counts_mine, BLOCK))
    return (new_loadings, new_noise)


def solution(mesh):
    return jax.shard_map(
        per_device,
        mesh=mesh,
        in_specs=(P("sens", "tm"), P("sens", None), P("sens"), P("tm", None), P()),
        out_specs=(P(("sens", "tm"), None), P(("sens", "tm"))),
        check_vma=False,
    )
```

```python
import jax
import jax.numpy as jnp
from jax import lax
from jax.experimental import pallas as pl
from jax.experimental.pallas import tpu as pltpu
from jax.sharding import PartitionSpec as P

BLOCK = 128


HIGH = lax.Precision.HIGHEST


def compose(before_seg, after_seg):
    return (before_seg[0] * after_seg[0], after_seg[0] * before_seg[1] + after_seg[1])


def _gauss_jordan(a_ref, o_ref):
    batch, n, _ = a_ref.shape
    lane = lax.broadcasted_iota(jnp.int32, (1, 1, n), 2)
    sub = lax.broadcasted_iota(jnp.int32, (1, n, 1), 1)

    def update(k, a):
        colmask = lane == k
        rowmask = sub == k
        c = jnp.sum(jnp.where(colmask, a, 0.0), axis=2, keepdims=True)
        r = jnp.sum(jnp.where(rowmask, a, 0.0), axis=1, keepdims=True)
        p = jnp.sum(jnp.where(colmask, r, 0.0), axis=2, keepdims=True)
        inv_p = 1.0 / p
        rs = jnp.where(colmask, inv_p, r * inv_p)
        out = jnp.where(colmask, -c * inv_p, a - c * rs)
        return jnp.where(rowmask, rs, out)

    if batch == 1:
        o_ref[...] = lax.fori_loop(0, n, update, a_ref[...], unroll=4)
    else:
        o_ref[...] = a_ref[...]

        def step(k, carry):
            o_ref[...] = update(k, o_ref[...])
            return carry

        lax.fori_loop(0, n, step, 0, unroll=2)


def spd_inverse(a):
    batch, n, _ = a.shape
    return pl.pallas_call(
        _gauss_jordan,
        out_shape=jax.ShapeDtypeStruct(a.shape, jnp.float32),
        in_specs=[pl.BlockSpec(memory_space=pltpu.VMEM)],
        out_specs=pl.BlockSpec(memory_space=pltpu.VMEM),
        cost_estimate=pl.CostEstimate(
            flops=8 * batch * n * n * n, transcendentals=0, bytes_accessed=8 * batch * n * n
        ),
    )(a)


def butterfly_sum(part, axis, count):
    distance = 1
    while distance < count:
        pairs = [(i, i ^ distance) for i in range(count)]
        part = part + lax.ppermute(part, axis, pairs)
        distance *= 2
    return part


def butterfly_gather(part, axis, count):
    place = lax.axis_index(axis)
    held = part[None]
    distance = 1
    while distance < count:
        pairs = [(i, i ^ distance) for i in range(count)]
        other = lax.ppermute(held, axis, pairs)
        upper = (place // distance) % 2 == 1
        held = jnp.where(
            upper, jnp.concatenate([other, held], 0), jnp.concatenate([held, other], 0)
        )
        distance *= 2
    return held


def entering(gains, values, position):
    inclusive = lax.associative_scan(compose, (gains, values), axis=0)
    shifted_value = jnp.concatenate([jnp.zeros_like(values[:1]), inclusive[1][:-1]], 0)
    return lax.dynamic_index_in_dim(shifted_value, position, 0, keepdims=True)


def per_device(observations, loadings, noise_var, decay, tiles):
    sens_count = lax.axis_size("sens")
    time_count = lax.axis_size("tm")
    sens_index = lax.axis_index("sens")
    time_index = lax.axis_index("tm")
    sens_dev, window_len = observations.shape
    factors = loadings.shape[1]
    blocks_dev = sens_dev // BLOCK
    blocks_share = blocks_dev // time_count
    block_ids = sens_index * blocks_dev + jnp.arange(blocks_dev)
    block_hit = (tiles[:, 0][:, None] == block_ids[None, :]).astype(jnp.float32)
    window_hit = (tiles[:, 1][:, None] == jnp.arange(time_count)[None, :]).astype(jnp.float32)
    tile_mask = jnp.dot(block_hit.T, window_hit, precision=HIGH)
    present = lax.dynamic_index_in_dim(tile_mask, time_index, 1, keepdims=False)
    sensor_mask = jnp.repeat(present, BLOCK)
    obs_mine = lax.all_to_all(observations, "tm", 0, 1, tiled=True)
    weighted = loadings * (1.0 / noise_var)[:, None] * sensor_mask[:, None]
    scaled = weighted.astype(jnp.bfloat16)
    weighted_lo = (weighted - scaled.astype(jnp.float32)).astype(jnp.bfloat16)
    loadings_hi = loadings.astype(jnp.bfloat16)
    loadings_lo = (loadings - loadings_hi.astype(jnp.float32)).astype(jnp.bfloat16)
    split = lax.dot_general(
        jnp.concatenate([scaled, weighted_lo], 1),
        jnp.concatenate([loadings_hi, loadings_lo], 1),
        (((0,), (0,)), ((), ())),
        preferred_element_type=jnp.float32,
    )
    gram_part = (
        split[:factors, :factors] + split[:factors, factors:] + split[factors:, :factors]
    )
    information = butterfly_sum(gram_part, "sens", sens_count)
    info_part = lax.dot_general(
        observations, scaled, (((0,), (0,)), ((), ())), preferred_element_type=jnp.float32
    )
    info_vec = butterfly_sum(info_part, "sens", sens_count)
    identity = jnp.eye(factors, dtype=jnp.float32)
    covariance = spd_inverse((identity + information)[None])[0]
    local_est = jnp.dot(info_vec, covariance, precision=HIGH)
    fwd_gain, fwd_local = lax.associative_scan(compose, (decay, local_est), axis=0)
    back_gain, back_local = lax.associative_scan(
        compose, (jnp.flip(decay, 0), jnp.flip(local_est, 0)), axis=0
    )
    summary = jnp.concatenate(
        [fwd_gain[-1:], fwd_local[-1:], back_gain[-1:], back_local[-1:]], 0
    )
    windows = butterfly_gather(summary, "tm", time_count)
    enter_fwd = entering(windows[:, 0], windows[:, 1], time_index)
    enter_back = entering(
        jnp.flip(windows[:, 2], 0), jnp.flip(windows[:, 3], 0), time_count - 1 - time_index
    )
    back_gain = jnp.flip(back_gain, 0)
    back_local = jnp.flip(back_local, 0)
    forward = fwd_local + fwd_gain * enter_fwd
    backward = back_local + back_gain * enter_back
    smoothed = ((1.0 - decay) / (1.0 + decay) * (forward + backward - local_est)).astype(
        jnp.bfloat16
    )
    mask_mine = lax.dynamic_slice_in_dim(tile_mask, time_index * blocks_share, blocks_share, 0)
    squares = lax.dot_general(
        smoothed, smoothed, (((0,), (0,)), ((), ())), preferred_element_type=jnp.float32
    )
    moment = squares + window_len * covariance
    gathered = lax.all_gather(
        jnp.concatenate([smoothed.astype(jnp.float32), moment], 0), "tm", axis=0, tiled=False
    )
    smooth_all = gathered[:, :window_len].reshape(time_count * window_len, factors)
    all_moments = gathered[:, window_len:]
    mask_full = jnp.broadcast_to(
        mask_mine[:, None, :, None], (blocks_share, BLOCK, time_count, window_len)
    ).reshape(blocks_share * BLOCK, time_count * window_len)
    observed = obs_mine * mask_full.astype(jnp.bfloat16)
    sq_mine = jnp.sum(jnp.square(observed.astype(jnp.float32)), axis=1)
    cross_mine = jnp.dot(
        observed, smooth_all.astype(jnp.bfloat16), preferred_element_type=jnp.float32
    )
    moment_mine = jnp.einsum("bw,wij->bij", mask_mine, all_moments, precision=HIGH)
    counts_mine = jnp.sum(mask_mine, axis=1)
    cross_blocks = cross_mine.reshape(blocks_share, BLOCK, factors)
    inverse_mine = spd_inverse(moment_mine)
    new_loadings = jnp.einsum(
        "bsk,bjk->bsj", cross_blocks, inverse_mine, precision=HIGH
    ).reshape(blocks_share * BLOCK, factors)
    explained = jnp.sum(new_loadings * cross_mine, axis=1)
    new_noise = (sq_mine - explained) / (window_len * jnp.repeat(counts_mine, BLOCK))
    return (new_loadings, new_noise)


def solution(mesh):
    return jax.shard_map(
        per_device,
        mesh=mesh,
        in_specs=(P("sens", "tm"), P("sens", None), P("sens"), P("tm", None), P()),
        out_specs=(P(("sens", "tm"), None), P(("sens", "tm"))),
        check_vma=False,
    )
```

```python
import jax
import jax.numpy as jnp
from jax import lax
from jax.experimental import pallas as pl
from jax.experimental.pallas import tpu as pltpu
from jax.sharding import PartitionSpec as P

BLOCK = 128


HIGH = lax.Precision.HIGHEST


def compose(before_seg, after_seg):
    return (before_seg[0] * after_seg[0], after_seg[0] * before_seg[1] + after_seg[1])


def _gauss_jordan(a_ref, o_ref):
    batch, n, _ = a_ref.shape
    lane = lax.broadcasted_iota(jnp.int32, (1, 1, n), 2)
    sub = lax.broadcasted_iota(jnp.int32, (1, n, 1), 1)

    def update(k, a):
        colmask = lane == k
        rowmask = sub == k
        c = jnp.sum(jnp.where(colmask, a, 0.0), axis=2, keepdims=True)
        r = jnp.sum(jnp.where(rowmask, a, 0.0), axis=1, keepdims=True)
        p = jnp.sum(jnp.where(colmask, r, 0.0), axis=2, keepdims=True)
        inv_p = 1.0 / p
        rs = jnp.where(colmask, inv_p, r * inv_p)
        out = jnp.where(colmask, -c * inv_p, a - c * rs)
        return jnp.where(rowmask, rs, out)

    if batch == 1:
        o_ref[...] = lax.fori_loop(0, n, update, a_ref[...], unroll=4)
    else:
        o_ref[...] = a_ref[...]
        pad = jnp.zeros((n - batch, n), jnp.float32)

        def step(k, carry):
            a = o_ref[...]
            colmask = lane == k
            rowmask = sub == k
            r = jnp.sum(jnp.where(rowmask, a, 0.0), axis=1)
            turned = jnp.transpose(jnp.concatenate([r, pad], 0))
            sign = jnp.where(sub < k, -1.0, 1.0)
            c = jnp.stack([turned[:, b : b + 1] for b in range(batch)], 0) * sign
            r = r[:, None, :]
            p = jnp.sum(jnp.where(colmask, r, 0.0), axis=2, keepdims=True)
            inv_p = 1.0 / p
            rs = jnp.where(colmask, inv_p, r * inv_p)
            out = jnp.where(colmask, -c * inv_p, a - c * rs)
            o_ref[...] = jnp.where(rowmask, rs, out)
            return carry

        lax.fori_loop(0, n, step, 0, unroll=2)


def spd_inverse(a):
    batch, n, _ = a.shape
    return pl.pallas_call(
        _gauss_jordan,
        out_shape=jax.ShapeDtypeStruct(a.shape, jnp.float32),
        in_specs=[pl.BlockSpec(memory_space=pltpu.VMEM)],
        out_specs=pl.BlockSpec(memory_space=pltpu.VMEM),
        cost_estimate=pl.CostEstimate(
            flops=8 * batch * n * n * n, transcendentals=0, bytes_accessed=8 * batch * n * n
        ),
    )(a)


def butterfly_sum(part, axis, count):
    distance = 1
    while distance < count:
        pairs = [(i, i ^ distance) for i in range(count)]
        part = part + lax.ppermute(part, axis, pairs)
        distance *= 2
    return part


def butterfly_gather(part, axis, count):
    place = lax.axis_index(axis)
    held = part[None]
    distance = 1
    while distance < count:
        pairs = [(i, i ^ distance) for i in range(count)]
        other = lax.ppermute(held, axis, pairs)
        upper = (place // distance) % 2 == 1
        held = jnp.where(
            upper, jnp.concatenate([other, held], 0), jnp.concatenate([held, other], 0)
        )
        distance *= 2
    return held


def entering(gains, values, position):
    inclusive = lax.associative_scan(compose, (gains, values), axis=0)
    shifted_value = jnp.concatenate([jnp.zeros_like(values[:1]), inclusive[1][:-1]], 0)
    return lax.dynamic_index_in_dim(shifted_value, position, 0, keepdims=True)


def per_device(observations, loadings, noise_var, decay, tiles):
    sens_count = lax.axis_size("sens")
    time_count = lax.axis_size("tm")
    sens_index = lax.axis_index("sens")
    time_index = lax.axis_index("tm")
    sens_dev, window_len = observations.shape
    factors = loadings.shape[1]
    blocks_dev = sens_dev // BLOCK
    blocks_share = blocks_dev // time_count
    block_ids = sens_index * blocks_dev + jnp.arange(blocks_dev)
    block_hit = (tiles[:, 0][:, None] == block_ids[None, :]).astype(jnp.float32)
    window_hit = (tiles[:, 1][:, None] == jnp.arange(time_count)[None, :]).astype(jnp.float32)
    tile_mask = jnp.dot(block_hit.T, window_hit, precision=HIGH)
    present = lax.dynamic_index_in_dim(tile_mask, time_index, 1, keepdims=False)
    sensor_mask = jnp.repeat(present, BLOCK)
    obs_mine = lax.all_to_all(observations, "tm", 0, 1, tiled=True)
    weighted = loadings * (1.0 / noise_var)[:, None] * sensor_mask[:, None]
    scaled = weighted.astype(jnp.bfloat16)
    weighted_lo = (weighted - scaled.astype(jnp.float32)).astype(jnp.bfloat16)
    loadings_hi = loadings.astype(jnp.bfloat16)
    loadings_lo = (loadings - loadings_hi.astype(jnp.float32)).astype(jnp.bfloat16)
    split = lax.dot_general(
        jnp.concatenate([scaled, weighted_lo], 1),
        jnp.concatenate([loadings_hi, loadings_lo], 1),
        (((0,), (0,)), ((), ())),
        preferred_element_type=jnp.float32,
    )
    gram_part = (
        split[:factors, :factors] + split[:factors, factors:] + split[factors:, :factors]
    )
    information = butterfly_sum(gram_part, "sens", sens_count)
    info_part = lax.dot_general(
        observations, scaled, (((0,), (0,)), ((), ())), preferred_element_type=jnp.float32
    )
    info_vec = butterfly_sum(info_part, "sens", sens_count)
    identity = jnp.eye(factors, dtype=jnp.float32)
    covariance = spd_inverse((identity + information)[None])[0]
    local_est = jnp.dot(info_vec, covariance, precision=HIGH)
    fwd_gain, fwd_local = lax.associative_scan(compose, (decay, local_est), axis=0)
    back_gain, back_local = lax.associative_scan(
        compose, (jnp.flip(decay, 0), jnp.flip(local_est, 0)), axis=0
    )
    summary = jnp.concatenate(
        [fwd_gain[-1:], fwd_local[-1:], back_gain[-1:], back_local[-1:]], 0
    )
    windows = butterfly_gather(summary, "tm", time_count)
    enter_fwd = entering(windows[:, 0], windows[:, 1], time_index)
    enter_back = entering(
        jnp.flip(windows[:, 2], 0), jnp.flip(windows[:, 3], 0), time_count - 1 - time_index
    )
    back_gain = jnp.flip(back_gain, 0)
    back_local = jnp.flip(back_local, 0)
    forward = fwd_local + fwd_gain * enter_fwd
    backward = back_local + back_gain * enter_back
    smoothed = ((1.0 - decay) / (1.0 + decay) * (forward + backward - local_est)).astype(
        jnp.bfloat16
    )
    mask_mine = lax.dynamic_slice_in_dim(tile_mask, time_index * blocks_share, blocks_share, 0)
    squares = lax.dot_general(
        smoothed, smoothed, (((0,), (0,)), ((), ())), preferred_element_type=jnp.float32
    )
    moment = squares + window_len * covariance
    gathered = lax.all_gather(
        jnp.concatenate([smoothed.astype(jnp.float32), moment], 0), "tm", axis=0, tiled=False
    )
    smooth_all = gathered[:, :window_len].reshape(time_count * window_len, factors)
    all_moments = gathered[:, window_len:]
    mask_full = jnp.broadcast_to(
        mask_mine[:, None, :, None], (blocks_share, BLOCK, time_count, window_len)
    ).reshape(blocks_share * BLOCK, time_count * window_len)
    observed = obs_mine * mask_full.astype(jnp.bfloat16)
    sq_mine = jnp.sum(jnp.square(observed.astype(jnp.float32)), axis=1)
    cross_mine = jnp.dot(
        observed, smooth_all.astype(jnp.bfloat16), preferred_element_type=jnp.float32
    )
    moment_mine = jnp.einsum("bw,wij->bij", mask_mine, all_moments, precision=HIGH)
    counts_mine = jnp.sum(mask_mine, axis=1)
    cross_blocks = cross_mine.reshape(blocks_share, BLOCK, factors)
    inverse_mine = spd_inverse(moment_mine)
    new_loadings = jnp.einsum(
        "bsk,bjk->bsj", cross_blocks, inverse_mine, precision=HIGH
    ).reshape(blocks_share * BLOCK, factors)
    explained = jnp.sum(new_loadings * cross_mine, axis=1)
    new_noise = (sq_mine - explained) / (window_len * jnp.repeat(counts_mine, BLOCK))
    return (new_loadings, new_noise)


def solution(mesh):
    return jax.shard_map(
        per_device,
        mesh=mesh,
        in_specs=(P("sens", "tm"), P("sens", None), P("sens"), P("tm", None), P()),
        out_specs=(P(("sens", "tm"), None), P(("sens", "tm"))),
        check_vma=False,
    )
```

```python
import jax
import jax.numpy as jnp
from jax import lax
from jax.experimental import pallas as pl
from jax.experimental.pallas import tpu as pltpu
from jax.sharding import PartitionSpec as P

BLOCK = 128


HIGH = lax.Precision.HIGHEST


def compose(before_seg, after_seg):
    return (before_seg[0] * after_seg[0], after_seg[0] * before_seg[1] + after_seg[1])


def _gauss_jordan(a_ref, o_ref):
    batch, n, _ = a_ref.shape
    lane = lax.broadcasted_iota(jnp.int32, (1, 1, n), 2)
    sub = lax.broadcasted_iota(jnp.int32, (1, n, 1), 1)

    def update(k, a):
        colmask = lane == k
        rowmask = sub == k
        c = jnp.sum(jnp.where(colmask, a, 0.0), axis=2, keepdims=True)
        r = jnp.sum(jnp.where(rowmask, a, 0.0), axis=1, keepdims=True)
        p = jnp.sum(jnp.where(colmask, r, 0.0), axis=2, keepdims=True)
        inv_p = 1.0 / p
        rs = jnp.where(colmask, inv_p, r * inv_p)
        out = jnp.where(colmask, -c * inv_p, a - c * rs)
        return jnp.where(rowmask, rs, out)

    if batch == 1:
        o_ref[...] = lax.fori_loop(0, n, update, a_ref[...], unroll=8)
    else:
        o_ref[...] = a_ref[...]

        def step(k, carry):
            o_ref[...] = update(k, o_ref[...])
            return carry

        lax.fori_loop(0, n, step, 0, unroll=4)


def spd_inverse(a):
    batch, n, _ = a.shape
    return pl.pallas_call(
        _gauss_jordan,
        out_shape=jax.ShapeDtypeStruct(a.shape, jnp.float32),
        in_specs=[pl.BlockSpec(memory_space=pltpu.VMEM)],
        out_specs=pl.BlockSpec(memory_space=pltpu.VMEM),
        cost_estimate=pl.CostEstimate(
            flops=8 * batch * n * n * n, transcendentals=0, bytes_accessed=8 * batch * n * n
        ),
    )(a)


def butterfly_sum(part, axis, count):
    distance = 1
    while distance < count:
        pairs = [(i, i ^ distance) for i in range(count)]
        part = part + lax.ppermute(part, axis, pairs)
        distance *= 2
    return part


def butterfly_gather(part, axis, count):
    place = lax.axis_index(axis)
    held = part[None]
    distance = 1
    while distance < count:
        pairs = [(i, i ^ distance) for i in range(count)]
        other = lax.ppermute(held, axis, pairs)
        upper = (place // distance) % 2 == 1
        held = jnp.where(
            upper, jnp.concatenate([other, held], 0), jnp.concatenate([held, other], 0)
        )
        distance *= 2
    return held


def entering(gains, values, position):
    inclusive = lax.associative_scan(compose, (gains, values), axis=0)
    shifted_value = jnp.concatenate([jnp.zeros_like(values[:1]), inclusive[1][:-1]], 0)
    return lax.dynamic_index_in_dim(shifted_value, position, 0, keepdims=True)


def per_device(observations, loadings, noise_var, decay, tiles):
    sens_count = lax.axis_size("sens")
    time_count = lax.axis_size("tm")
    sens_index = lax.axis_index("sens")
    time_index = lax.axis_index("tm")
    sens_dev, window_len = observations.shape
    factors = loadings.shape[1]
    blocks_dev = sens_dev // BLOCK
    blocks_share = blocks_dev // time_count
    block_ids = sens_index * blocks_dev + jnp.arange(blocks_dev)
    block_hit = (tiles[:, 0][:, None] == block_ids[None, :]).astype(jnp.float32)
    window_hit = (tiles[:, 1][:, None] == jnp.arange(time_count)[None, :]).astype(jnp.float32)
    tile_mask = jnp.dot(block_hit.T, window_hit, precision=HIGH)
    present = lax.dynamic_index_in_dim(tile_mask, time_index, 1, keepdims=False)
    sensor_mask = jnp.repeat(present, BLOCK)
    obs_mine = lax.all_to_all(observations, "tm", 0, 1, tiled=True)
    weighted = loadings * (1.0 / noise_var)[:, None] * sensor_mask[:, None]
    scaled = weighted.astype(jnp.bfloat16)
    weighted_lo = (weighted - scaled.astype(jnp.float32)).astype(jnp.bfloat16)
    loadings_hi = loadings.astype(jnp.bfloat16)
    loadings_lo = (loadings - loadings_hi.astype(jnp.float32)).astype(jnp.bfloat16)
    split = lax.dot_general(
        jnp.concatenate([scaled, weighted_lo], 1),
        jnp.concatenate([loadings_hi, loadings_lo], 1),
        (((0,), (0,)), ((), ())),
        preferred_element_type=jnp.float32,
    )
    gram_part = (
        split[:factors, :factors] + split[:factors, factors:] + split[factors:, :factors]
    )
    information = butterfly_sum(gram_part, "sens", sens_count)
    info_part = lax.dot_general(
        observations, scaled, (((0,), (0,)), ((), ())), preferred_element_type=jnp.float32
    )
    info_vec = butterfly_sum(info_part, "sens", sens_count)
    identity = jnp.eye(factors, dtype=jnp.float32)
    covariance = spd_inverse((identity + information)[None])[0]
    local_est = jnp.dot(info_vec, covariance, precision=HIGH)
    fwd_gain, fwd_local = lax.associative_scan(compose, (decay, local_est), axis=0)
    back_gain, back_local = lax.associative_scan(
        compose, (jnp.flip(decay, 0), jnp.flip(local_est, 0)), axis=0
    )
    summary = jnp.concatenate(
        [fwd_gain[-1:], fwd_local[-1:], back_gain[-1:], back_local[-1:]], 0
    )
    windows = butterfly_gather(summary, "tm", time_count)
    enter_fwd = entering(windows[:, 0], windows[:, 1], time_index)
    enter_back = entering(
        jnp.flip(windows[:, 2], 0), jnp.flip(windows[:, 3], 0), time_count - 1 - time_index
    )
    back_gain = jnp.flip(back_gain, 0)
    back_local = jnp.flip(back_local, 0)
    forward = fwd_local + fwd_gain * enter_fwd
    backward = back_local + back_gain * enter_back
    smoothed = ((1.0 - decay) / (1.0 + decay) * (forward + backward - local_est)).astype(
        jnp.bfloat16
    )
    mask_mine = lax.dynamic_slice_in_dim(tile_mask, time_index * blocks_share, blocks_share, 0)
    squares = lax.dot_general(
        smoothed, smoothed, (((0,), (0,)), ((), ())), preferred_element_type=jnp.float32
    )
    moment = squares + window_len * covariance
    gathered = lax.all_gather(
        jnp.concatenate([smoothed.astype(jnp.float32), moment], 0), "tm", axis=0, tiled=False
    )
    smooth_all = gathered[:, :window_len].reshape(time_count * window_len, factors)
    all_moments = gathered[:, window_len:]
    mask_full = jnp.broadcast_to(
        mask_mine[:, None, :, None], (blocks_share, BLOCK, time_count, window_len)
    ).reshape(blocks_share * BLOCK, time_count * window_len)
    observed = obs_mine * mask_full.astype(jnp.bfloat16)
    sq_mine = jnp.sum(jnp.square(observed.astype(jnp.float32)), axis=1)
    cross_mine = jnp.dot(
        observed, smooth_all.astype(jnp.bfloat16), preferred_element_type=jnp.float32
    )
    moment_mine = jnp.einsum("bw,wij->bij", mask_mine, all_moments, precision=HIGH)
    counts_mine = jnp.sum(mask_mine, axis=1)
    cross_blocks = cross_mine.reshape(blocks_share, BLOCK, factors)
    inverse_mine = spd_inverse(moment_mine)
    new_loadings = jnp.einsum(
        "bsk,bjk->bsj", cross_blocks, inverse_mine, precision=HIGH
    ).reshape(blocks_share * BLOCK, factors)
    explained = jnp.sum(new_loadings * cross_mine, axis=1)
    new_noise = (sq_mine - explained) / (window_len * jnp.repeat(counts_mine, BLOCK))
    return (new_loadings, new_noise)


def solution(mesh):
    return jax.shard_map(
        per_device,
        mesh=mesh,
        in_specs=(P("sens", "tm"), P("sens", None), P("sens"), P("tm", None), P()),
        out_specs=(P(("sens", "tm"), None), P(("sens", "tm"))),
        check_vma=False,
    )
```
